256 devices in a mesh: section: 16 (over z_lo, x, core), tp: 16 (over y, z_hi).
Axes of the slice: x: 4, y: 4, z: 8 (z_hi: 4, z_lo: 2; z = z_hi * 2 + z_lo), core: 2. Of those that a mesh axis runs over, the one named last changes fastest.
Arguments:
- tokens: bfloat16 [2, 512, 4096], P(None, 'tp'), may hold values from -6 to 6
- norm_gains: float32 [2, 4096], replicated, may hold values from 0.1 to 1.9
- w_gate: bfloat16 [16, 4096, 2048], P('section', None, 'tp'), may hold values from -0.09375 to 0.09375
- w_up: bfloat16 [16, 4096, 2048], P('section', None, 'tp'), may hold values from -0.09375 to 0.09375
- w_down: bfloat16 [16, 2048, 4096], P('section', 'tp'), may hold values from -0.0625 to 0.0625
Outputs:
- acts: bfloat16 [16, 2, 512, 512], P('section', None, 'tp')
The draws below stay inside these ranges and needn't reach their ends.
All inputs are finite; a program needn't handle non-finite values.
Results may differ from the reference program's by a relative error of at most 0.022.
Values may be sent and summed in bfloat16 or wider, within the bound.
No kernel may reach another device: no remote copies, remote signals or barrier semaphores. Data moves between devices by JAX's collectives and lax.ppermute only.
A program may use at most 64 MiB of HBM per device.

```python
import jax
import jax.numpy as jnp
from jax import lax

D = 4096
FF = 16384
MICRO = 2
LAYERS = 2
SPLIT = 8
PIECE_FF = 2048
PIECE_D = 512
TOKENS = 512
N_TP = 16


def raised(values, stream_key, source, target, blocks, factor):
    owner, partner = [(jnp.arange(values.shape[axis_at]) // (values.shape[axis_at] // blocks)).reshape([-1 if axis == axis_at else 1 for axis in range(values.ndim)]) for axis_at in (source, target)]
    chosen = jax.random.permutation(stream_key, blocks)[partner]
    strong = (owner == chosen) | (owner == (partner + blocks // 2) % blocks)
    return jnp.where(strong, factor * values, values)


def shard_levels(own_key, shape, split, low, top_value):
    def one(axis_at, blocks):
        draws = jax.random.uniform(jax.random.fold_in(jax.random.fold_in(own_key, 6), axis_at), (blocks,), jnp.float32, low / len(split), top_value / len(split))
        return jnp.repeat(jnp.exp(draws), shape[axis_at] // blocks).reshape((-1,) + (1,) * (len(shape) - axis_at - 1))

    factor_of = one(*split[0])
    for cut in split[1:]:
        factor_of = factor_of * one(*cut)
    return factor_of


def noise(stream_key, dims, scale, bound, cuts=(), dtype=jnp.bfloat16):
    entries = jax.random.normal(stream_key, dims, jnp.float32) * scale
    if len(cuts) > 0:
        entries = shard_levels(stream_key, dims, cuts, -0.22, 0.18) * entries
    return jnp.clip(entries, min=-bound, max=bound).astype(dtype)


def gaussian_with(rng, dims, scale, reach, split, heavy, held_as=jnp.bfloat16):
    array = scale * jax.random.normal(rng, dims, jnp.float32)
    if split:
        array = array * shard_levels(rng, dims, split, -0.22, 0.18)
    return jnp.clip(raised(array, jax.random.fold_in(rng, 3), *heavy), -reach, reach).astype(held_as)


def setup_inputs(seed: int = 0) -> dict:
    key_of = jax.random.split(jax.random.key(seed), 6)
    tokens = noise(key_of[0], (MICRO, TOKENS, D), 1.0, 6.0, ((1, 16),))
    norm_gains = jnp.clip(1.0 + 0.18 * jax.random.normal(key_of[1], (LAYERS, D), jnp.float32), 0.1, 1.9)
    w_gate = noise(key_of[2], (LAYERS * SPLIT, D, PIECE_FF), D ** -0.5, 0.09375, ((0, 16), (2, 16)))
    w_up = noise(key_of[3], (LAYERS * SPLIT, D, PIECE_FF), D ** -0.5, 0.09375, ((0, 16), (2, 16)))
    w_down = gaussian_with(key_of[4], (LAYERS * SPLIT, PIECE_FF, D), FF ** -0.5, 0.0625, ((0, 16), (1, 16)), (1, 2, 16, 2.0))
    return dict(tokens=tokens, norm_gains=norm_gains, w_gate=w_gate, w_up=w_up, w_down=w_down)


epsilon = 1e-05

def block_sum(active, down_rows):
    run_count = SPLIT * N_TP
    block_width = active.shape[1] // run_count
    pieces = active.reshape(active.shape[0], run_count, block_width).transpose(1, 0, 2)
    down_pieces = down_rows.reshape(run_count, block_width, down_rows.shape[1])

    def add_piece(running, operands):
        block_term = jnp.dot(operands[0], operands[1], preferred_element_type=jnp.float32)
        rounded = lax.optimization_barrier(block_term.astype(jnp.bfloat16))
        return (running + rounded.astype(jnp.float32), None)
    start_sum = jnp.zeros((active.shape[0], down_rows.shape[1]), jnp.float32)
    running, _ = lax.scan(add_piece, start_sum, (pieces, down_pieces))
    return running

def reference(tokens, norm_gains, w_gate, w_up, w_down):
    hidden_rows = tokens.reshape(-1, D)
    outputs = []
    for layer_index in range(LAYERS):
        first = SPLIT * layer_index
        gate_cols = jnp.concatenate([w_gate[first + k] for k in range(SPLIT)], axis=1)
        up_cols = jnp.concatenate([w_up[first + k] for k in range(SPLIT)], axis=1)
        down_rows = jnp.concatenate([w_down[first + k] for k in range(SPLIT)], axis=0)
        current = hidden_rows.astype(jnp.float32)
        inv_rms = lax.rsqrt(lax.optimization_barrier(jnp.mean(current * current, axis=1, keepdims=True)) + epsilon)
        normed = (current * inv_rms * norm_gains[layer_index]).astype(jnp.bfloat16)
        gate_proj = jnp.dot(normed, gate_cols, preferred_element_type=jnp.float32)
        up_proj = jnp.dot(normed, up_cols, preferred_element_type=jnp.float32)
        active = (jax.nn.silu(gate_proj) * up_proj).astype(jnp.bfloat16)
        summed = block_sum(active, down_rows)
        hidden_rows = (current + summed).astype(jnp.bfloat16)
        shaped = hidden_rows.reshape(MICRO, TOKENS, D)
        for k in range(SPLIT):
            outputs.append(shaped[:, :, k * PIECE_D:(k + 1) * PIECE_D])
    return jnp.stack(outputs, axis=0)
```

```python
import jax
import jax.numpy as jnp
from jax import lax
from jax.sharding import PartitionSpec as P

LAYERS = 2
PIECES = 1


epsilon = 1e-05


def swapped(value, axis, mask):
    pairs = [(source, source ^ mask) for source in range(lax.axis_size(axis))]
    return lax.ppermute(value, axis, pairs)


def shifted(value, axis, steps):
    count = lax.axis_size(axis)
    return lax.ppermute(value, axis, [(source, source + steps) for source in range(count - steps)])


def body(tokens, norm_gains, w_gate, w_up, w_down):
    section_count = lax.axis_size("section")
    split = section_count // LAYERS
    bit_count = split.bit_length() - 1
    position = lax.axis_index("section")
    section_layer = position // split
    member = position % split
    core = member % 2
    xpos = member // 2
    x_count = split // 2

    micro_count, tok_dev, model_width = tokens.shape
    piece_width = model_width // split
    half_width = model_width // 2
    row_count = tok_dev // PIECES
    piece_count = micro_count * PIECES
    tick_count = piece_count + LAYERS - 1

    def pick(value, axis, which):
        shape = value.shape
        grouped = value.reshape(shape[:axis] + (x_count, 2, piece_width) + shape[axis + 1:])
        chosen = lax.dynamic_index_in_dim(grouped, which, axis + 1, keepdims=False)
        return chosen.reshape(shape[:axis] + (half_width,) + shape[axis + 1:])

    other = 1 - core
    gate_own = pick(w_gate[0], 0, core)
    gate_other = pick(w_gate[0], 0, other)
    up_own = pick(w_up[0], 0, core)
    up_other = pick(w_up[0], 0, other)
    down_own = pick(w_down[0], 1, core)
    down_other = pick(w_down[0], 1, other)
    norm_gain = lax.dynamic_index_in_dim(norm_gains, section_layer, 0, keepdims=False)
    gain_own = pick(norm_gain, 0, core)

    def from_tokens(piece_index):
        micro_index, part = divmod(piece_index, PIECES)
        rows = tokens[micro_index, part * row_count:(part + 1) * row_count].astype(jnp.float32)
        return pick(rows, 1, core), jnp.sum(rows * rows, axis=1, keepdims=True)

    def from_received(received):
        current = received.astype(jnp.float32)
        own_sq = jnp.sum(current * current, axis=1, keepdims=True)
        return current, own_sq + swapped(own_sq, "section", 1)

    def tick(current, square_sum):
        inv_rms = lax.rsqrt(square_sum / model_width + epsilon)
        normed = (current * inv_rms * gain_own).astype(jnp.bfloat16)
        gathered = lax.all_gather(normed, "tp", axis=0, tiled=True)
        gathered_other = swapped(gathered, "section", 1)
        gate_proj = jnp.dot(gathered, gate_own, preferred_element_type=jnp.float32) + jnp.dot(
            gathered_other, gate_other, preferred_element_type=jnp.float32
        )
        up_proj = jnp.dot(gathered, up_own, preferred_element_type=jnp.float32) + jnp.dot(
            gathered_other, up_other, preferred_element_type=jnp.float32
        )
        active = (jax.nn.silu(gate_proj) * up_proj).astype(jnp.bfloat16)
        part_other = jnp.dot(active, down_other, preferred_element_type=jnp.float32).astype(jnp.bfloat16)
        part_from_other = swapped(part_other, "section", 1)
        part_own = jnp.dot(active, down_own, preferred_element_type=jnp.float32).astype(jnp.bfloat16)
        pair = (part_own.astype(jnp.float32) + part_from_other.astype(jnp.float32)).astype(jnp.bfloat16)
        summed = lax.psum_scatter(pair, "tp", scatter_dimension=0, tiled=True)
        for level in range(1, bit_count):
            summed = (
                summed.astype(jnp.float32) + swapped(summed, "section", 1 << level).astype(jnp.float32)
            )
            if level < bit_count - 1:
                summed = summed.astype(jnp.bfloat16)
        full_half = (current + summed.astype(jnp.float32)).astype(jnp.bfloat16)
        block = lax.dynamic_index_in_dim(
            full_half.reshape(row_count, x_count, piece_width), xpos, 1, keepdims=False
        )
        return full_half, block

    blocks = []
    received = None
    for tick_index in range(tick_count):
        if tick_index == 0:
            current, square_sum = from_tokens(0)
        elif tick_index >= piece_count:
            current, square_sum = from_received(received)
        else:
            first_current, first_sum = from_tokens(tick_index)
            later_current, later_sum = from_received(received)
            is_first = section_layer == 0
            current = jnp.where(is_first, first_current, later_current)
            square_sum = jnp.where(is_first, first_sum, later_sum)
        full_half, block = tick(current, square_sum)
        blocks.append(block)
        if tick_index < tick_count - 1:
            received = shifted(full_half, "section", split)

    stacked = jnp.stack(blocks, axis=0)
    outputs = []
    for micro_index in range(micro_count):
        parts = [
            lax.dynamic_index_in_dim(stacked, micro_index * PIECES + part + section_layer, 0, keepdims=False)
            for part in range(PIECES)
        ]
        outputs.append(jnp.concatenate(parts, axis=0))
    return jnp.stack(outputs, axis=0)[None]


def solution(mesh):
    in_specs = (
        P(None, "tp", None),
        P(),
        P("section", None, "tp"),
        P("section", None, "tp"),
        P("section", "tp", None),
    )
    out_specs = P("section", None, "tp", None)
    return jax.shard_map(body, mesh=mesh, in_specs=in_specs, out_specs=out_specs, check_vma=False)
```

```python
import jax
import jax.numpy as jnp
from jax import lax
from jax.sharding import PartitionSpec as P

LAYERS = 2
PIECES = 1


epsilon = 1e-05


def swapped(value, axis, mask):
    pairs = [(source, source ^ mask) for source in range(lax.axis_size(axis))]
    return lax.ppermute(value, axis, pairs)


def tp_ring(value, inner, outer, stage, step):
    pairs = []
    for source in range(inner * outer):
        high, low = divmod(source, inner)
        if stage == "inner":
            target = high * inner + (low + step) % inner
        else:
            target = ((high + step) % outer) * inner + low
        pairs.append((source, target))
    return lax.ppermute(value, "tp", pairs)


def ring_gather(block, ring):
    half = block.shape[1] // 2
    from_left = ring(block, 1)
    from_right = ring(block, -1)
    opposite = jnp.concatenate(
        [ring(from_left[:, :half], 1), ring(from_right[:, half:], -1)], axis=1
    )
    return jnp.concatenate([block, from_right, opposite, from_left], axis=0)


def ring_scatter(groups, ring):
    rows = groups.shape[0] // 4
    half = groups.shape[1] // 2
    own, plus, opposite, minus = (groups[i * rows:(i + 1) * rows] for i in range(4))
    early_left = ring(opposite[:, :half], 1).astype(jnp.float32)
    early_right = ring(opposite[:, half:], -1).astype(jnp.float32)
    to_right = jnp.concatenate(
        [(plus[:, :half].astype(jnp.float32) + early_left).astype(jnp.bfloat16), plus[:, half:]], axis=1
    )
    to_left = jnp.concatenate(
        [minus[:, :half], (minus[:, half:].astype(jnp.float32) + early_right).astype(jnp.bfloat16)], axis=1
    )
    return (
        own.astype(jnp.float32)
        + ring(to_right, 1).astype(jnp.float32)
        + ring(to_left, -1).astype(jnp.float32)
    )


def shifted(value, axis, steps):
    count = lax.axis_size(axis)
    return lax.ppermute(value, axis, [(source, source + steps) for source in range(count - steps)])


def body(tokens, norm_gains, w_gate, w_up, w_down):
    section_count = lax.axis_size("section")
    split = section_count // LAYERS
    bit_count = split.bit_length() - 1
    position = lax.axis_index("section")
    section_layer = position // split
    member = position % split
    core = member % 2
    xpos = member // 2
    x_count = split // 2

    tp_count = lax.axis_size("tp")
    inner = 4
    outer = tp_count // inner

    def inner_ring(value, step):
        return tp_ring(value, inner, outer, "inner", step)

    def outer_ring(value, step):
        return tp_ring(value, inner, outer, "outer", step)

    micro_count, tok_dev, model_width = tokens.shape
    piece_width = model_width // split
    half_width = model_width // 2
    row_count = tok_dev // PIECES
    piece_count = micro_count * PIECES
    tick_count = piece_count + LAYERS - 1

    def pick(value, axis, which):
        shape = value.shape
        grouped = value.reshape(shape[:axis] + (x_count, 2, piece_width) + shape[axis + 1:])
        chosen = lax.dynamic_index_in_dim(grouped, which, axis + 1, keepdims=False)
        return chosen.reshape(shape[:axis] + (half_width,) + shape[axis + 1:])

    other = 1 - core
    gate_own = pick(w_gate[0], 0, core)
    gate_other = pick(w_gate[0], 0, other)
    up_own = pick(w_up[0], 0, core)
    up_other = pick(w_up[0], 0, other)
    down_own = pick(w_down[0], 1, core)
    down_other = pick(w_down[0], 1, other)
    norm_gain = lax.dynamic_index_in_dim(norm_gains, section_layer, 0, keepdims=False)
    gain_own = pick(norm_gain, 0, core)

    def from_tokens(piece_index):
        micro_index, part = divmod(piece_index, PIECES)
        rows = tokens[micro_index, part * row_count:(part + 1) * row_count].astype(jnp.float32)
        return pick(rows, 1, core), jnp.sum(rows * rows, axis=1, keepdims=True)

    def from_received(received):
        current = received.astype(jnp.float32)
        own_sq = jnp.sum(current * current, axis=1, keepdims=True)
        return current, own_sq + swapped(own_sq, "section", 1)

    def tick(current, square_sum):
        inv_rms = lax.rsqrt(square_sum / model_width + epsilon)
        normed = (current * inv_rms * gain_own).astype(jnp.bfloat16)
        gathered = ring_gather(ring_gather(normed, inner_ring), outer_ring)
        gathered_other = swapped(gathered, "section", 1)
        gate_proj = jnp.dot(gathered, gate_own, preferred_element_type=jnp.float32) + jnp.dot(
            gathered_other, gate_other, preferred_element_type=jnp.float32
        )
        up_proj = jnp.dot(gathered, up_own, preferred_element_type=jnp.float32) + jnp.dot(
            gathered_other, up_other, preferred_element_type=jnp.float32
        )
        active = (jax.nn.silu(gate_proj) * up_proj).astype(jnp.bfloat16)
        part_other = jnp.dot(active, down_other, preferred_element_type=jnp.float32).astype(jnp.bfloat16)
        part_from_other = swapped(part_other, "section", 1)
        part_own = jnp.dot(active, down_own, preferred_element_type=jnp.float32).astype(jnp.bfloat16)
        pair = (part_own.astype(jnp.float32) + part_from_other.astype(jnp.float32)).astype(jnp.bfloat16)
        summed = ring_scatter(ring_scatter(pair, outer_ring).astype(jnp.bfloat16), inner_ring).astype(jnp.bfloat16)
        for level in range(1, bit_count):
            summed = (
                summed.astype(jnp.float32) + swapped(summed, "section", 1 << level).astype(jnp.float32)
            )
            if level < bit_count - 1:
                summed = summed.astype(jnp.bfloat16)
        full_half = (current + summed.astype(jnp.float32)).astype(jnp.bfloat16)
        block = lax.dynamic_index_in_dim(
            full_half.reshape(row_count, x_count, piece_width), xpos, 1, keepdims=False
        )
        return full_half, block

    blocks = []
    received = None
    for tick_index in range(tick_count):
        if tick_index == 0:
            current, square_sum = from_tokens(0)
        elif tick_index >= piece_count:
            current, square_sum = from_received(received)
        else:
            first_current, first_sum = from_tokens(tick_index)
            later_current, later_sum = from_received(received)
            is_first = section_layer == 0
            current = jnp.where(is_first, first_current, later_current)
            square_sum = jnp.where(is_first, first_sum, later_sum)
        full_half, block = tick(current, square_sum)
        blocks.append(block)
        if tick_index < tick_count - 1:
            received = shifted(full_half, "section", split)

    stacked = jnp.stack(blocks, axis=0)
    outputs = []
    for micro_index in range(micro_count):
        parts = [
            lax.dynamic_index_in_dim(stacked, micro_index * PIECES + part + section_layer, 0, keepdims=False)
            for part in range(PIECES)
        ]
        outputs.append(jnp.concatenate(parts, axis=0))
    return jnp.stack(outputs, axis=0)[None]


def solution(mesh):
    in_specs = (
        P(None, "tp", None),
        P(),
        P("section", None, "tp"),
        P("section", None, "tp"),
        P("section", "tp", None),
    )
    out_specs = P("section", None, "tp", None)
    return jax.shard_map(body, mesh=mesh, in_specs=in_specs, out_specs=out_specs, check_vma=False)
```

```python
import jax
import jax.numpy as jnp
from jax import lax
from jax.sharding import PartitionSpec as P

LAYERS = 2
PIECES = 1


epsilon = 1e-05


def swapped(value, axis, mask):
    pairs = [(source, source ^ mask) for source in range(lax.axis_size(axis))]
    return lax.ppermute(value, axis, pairs)


def tp_ring(value, inner, outer, stage, step):
    pairs = []
    for source in range(inner * outer):
        high, low = divmod(source, inner)
        if stage == "inner":
            target = high * inner + (low + step) % inner
        else:
            target = ((high + step) % outer) * inner + low
        pairs.append((source, target))
    return lax.ppermute(value, "tp", pairs)


def ring_gather(block, ring):
    half = block.shape[1] // 2
    from_left = ring(block, 1)
    from_right = ring(block, -1)
    opposite = jnp.concatenate(
        [ring(from_left[:, :half], 1), ring(from_right[:, half:], -1)], axis=1
    )
    return jnp.concatenate([block, from_right, opposite, from_left], axis=0)


def ring_scatter(groups, ring):
    rows = groups.shape[0] // 4
    half = groups.shape[1] // 2
    own, plus, opposite, minus = (groups[i * rows:(i + 1) * rows] for i in range(4))
    early_left = ring(opposite[:, :half], 1).astype(jnp.float32)
    early_right = ring(opposite[:, half:], -1).astype(jnp.float32)
    to_right = jnp.concatenate(
        [(plus[:, :half].astype(jnp.float32) + early_left).astype(jnp.bfloat16), plus[:, half:]], axis=1
    )
    to_left = jnp.concatenate(
        [minus[:, :half], (minus[:, half:].astype(jnp.float32) + early_right).astype(jnp.bfloat16)], axis=1
    )
    return (
        own.astype(jnp.float32)
        + ring(to_right, 1).astype(jnp.float32)
        + ring(to_left, -1).astype(jnp.float32)
    )


def direct_gather(block, ring):
    return jnp.concatenate([block, ring(block, -1), ring(block, 2), ring(block, 1)], axis=0)


def direct_scatter(groups, ring):
    rows = groups.shape[0] // 4
    own, plus, opposite, minus = (groups[i * rows:(i + 1) * rows] for i in range(4))
    return (
        own.astype(jnp.float32)
        + ring(plus, 1).astype(jnp.float32)
        + ring(opposite, 2).astype(jnp.float32)
        + ring(minus, -1).astype(jnp.float32)
    )


def shifted(value, axis, steps):
    count = lax.axis_size(axis)
    return lax.ppermute(value, axis, [(source, source + steps) for source in range(count - steps)])


def body(tokens, norm_gains, w_gate, w_up, w_down):
    section_count = lax.axis_size("section")
    split = section_count // LAYERS
    bit_count = split.bit_length() - 1
    position = lax.axis_index("section")
    section_layer = position // split
    member = position % split
    core = member % 2
    xpos = member // 2
    x_count = split // 2

    tp_count = lax.axis_size("tp")
    inner = 4
    outer = tp_count // inner

    def inner_ring(value, step):
        return tp_ring(value, inner, outer, "inner", step)

    def outer_ring(value, step):
        return tp_ring(value, inner, outer, "outer", step)

    micro_count, tok_dev, model_width = tokens.shape
    piece_width = model_width // split
    half_width = model_width // 2
    row_count = tok_dev // PIECES
    piece_count = micro_count * PIECES
    tick_count = piece_count + LAYERS - 1

    def pick(value, axis, which):
        shape = value.shape
        grouped = value.reshape(shape[:axis] + (x_count, 2, piece_width) + shape[axis + 1:])
        chosen = lax.dynamic_index_in_dim(grouped, which, axis + 1, keepdims=False)
        return chosen.reshape(shape[:axis] + (half_width,) + shape[axis + 1:])

    other = 1 - core
    gate_own = pick(w_gate[0], 0, core)
    gate_other = pick(w_gate[0], 0, other)
    up_own = pick(w_up[0], 0, core)
    up_other = pick(w_up[0], 0, other)
    down_own = pick(w_down[0], 1, core)
    down_other = pick(w_down[0], 1, other)
    norm_gain = lax.dynamic_index_in_dim(norm_gains, section_layer, 0, keepdims=False)
    gain_own = pick(norm_gain, 0, core)

    def from_tokens(piece_index):
        micro_index, part = divmod(piece_index, PIECES)
        rows = tokens[micro_index, part * row_count:(part + 1) * row_count].astype(jnp.float32)
        return pick(rows, 1, core), jnp.sum(rows * rows, axis=1, keepdims=True)

    def from_received(received):
        current = received.astype(jnp.float32)
        own_sq = jnp.sum(current * current, axis=1, keepdims=True)
        return current, own_sq + swapped(own_sq, "section", 1)

    def tick(current, square_sum):
        inv_rms = lax.rsqrt(square_sum / model_width + epsilon)
        normed = (current * inv_rms * gain_own).astype(jnp.bfloat16)
        gathered = ring_gather(direct_gather(normed, inner_ring), outer_ring)
        gathered_other = swapped(gathered, "section", 1)
        gate_proj = jnp.dot(gathered, gate_own, preferred_element_type=jnp.float32) + jnp.dot(
            gathered_other, gate_other, preferred_element_type=jnp.float32
        )
        up_proj = jnp.dot(gathered, up_own, preferred_element_type=jnp.float32) + jnp.dot(
            gathered_other, up_other, preferred_element_type=jnp.float32
        )
        active = (jax.nn.silu(gate_proj) * up_proj).astype(jnp.bfloat16)
        part_other = jnp.dot(active, down_other, preferred_element_type=jnp.float32).astype(jnp.bfloat16)
        part_from_other = swapped(part_other, "section", 1)
        part_own = jnp.dot(active, down_own, preferred_element_type=jnp.float32).astype(jnp.bfloat16)
        pair = (part_own.astype(jnp.float32) + part_from_other.astype(jnp.float32)).astype(jnp.bfloat16)
        summed = direct_scatter(ring_scatter(pair, outer_ring).astype(jnp.bfloat16), inner_ring).astype(jnp.bfloat16)
        summed = summed.astype(jnp.float32) + sum(
            swapped(summed, "section", 2 * mask).astype(jnp.float32) for mask in range(1, x_count)
        )
        full_half = (current + summed.astype(jnp.float32)).astype(jnp.bfloat16)
        block = lax.dynamic_index_in_dim(
            full_half.reshape(row_count, x_count, piece_width), xpos, 1, keepdims=False
        )
        return full_half, block

    blocks = []
    received = None
    for tick_index in range(tick_count):
        if tick_index == 0:
            current, square_sum = from_tokens(0)
        elif tick_index >= piece_count:
            current, square_sum = from_received(received)
        else:
            first_current, first_sum = from_tokens(tick_index)
            later_current, later_sum = from_received(received)
            is_first = section_layer == 0
            current = jnp.where(is_first, first_current, later_current)
            square_sum = jnp.where(is_first, first_sum, later_sum)
        full_half, block = tick(current, square_sum)
        blocks.append(block)
        if tick_index < tick_count - 1:
            received = shifted(full_half, "section", split)

    stacked = jnp.stack(blocks, axis=0)
    outputs = []
    for micro_index in range(micro_count):
        parts = [
            lax.dynamic_index_in_dim(stacked, micro_index * PIECES + part + section_layer, 0, keepdims=False)
            for part in range(PIECES)
        ]
        outputs.append(jnp.concatenate(parts, axis=0))
    return jnp.stack(outputs, axis=0)[None]


def solution(mesh):
    in_specs = (
        P(None, "tp", None),
        P(),
        P("section", None, "tp"),
        P("section", None, "tp"),
        P("section", "tp", None),
    )
    out_specs = P("section", None, "tp", None)
    return jax.shard_map(body, mesh=mesh, in_specs=in_specs, out_specs=out_specs, check_vma=False)
```

```python
import jax
import jax.numpy as jnp
from jax import lax
from jax.sharding import PartitionSpec as P

LAYERS = 2


epsilon = 1e-05


def swapped(value, axis, mask):
    pairs = [(source, source ^ mask) for source in range(lax.axis_size(axis))]
    return lax.ppermute(value, axis, pairs)


def tp_ring(value, inner, outer, stage, step):
    pairs = []
    for source in range(inner * outer):
        high, low = divmod(source, inner)
        if stage == "inner":
            target = high * inner + (low + step) % inner
        else:
            target = ((high + step) % outer) * inner + low
        pairs.append((source, target))
    return lax.ppermute(value, "tp", pairs)


def ring_gather(block, ring):
    half = block.shape[1] // 2
    from_left = ring(block, 1)
    from_right = ring(block, -1)
    opposite = jnp.concatenate(
        [ring(from_left[:, :half], 1), ring(from_right[:, half:], -1)], axis=1
    )
    return jnp.concatenate([block, from_right, opposite, from_left], axis=0)


def ring_scatter(groups, ring):
    rows = groups.shape[0] // 4
    half = groups.shape[1] // 2
    own, plus, opposite, minus = (groups[i * rows:(i + 1) * rows] for i in range(4))
    early_left = ring(opposite[:, :half], 1).astype(jnp.float32)
    early_right = ring(opposite[:, half:], -1).astype(jnp.float32)
    to_right = jnp.concatenate(
        [(plus[:, :half].astype(jnp.float32) + early_left).astype(jnp.bfloat16), plus[:, half:]], axis=1
    )
    to_left = jnp.concatenate(
        [minus[:, :half], (minus[:, half:].astype(jnp.float32) + early_right).astype(jnp.bfloat16)], axis=1
    )
    return (
        own.astype(jnp.float32)
        + ring(to_right, 1).astype(jnp.float32)
        + ring(to_left, -1).astype(jnp.float32)
    )


def direct_gather(block, ring):
    return jnp.concatenate([block, ring(block, -1), ring(block, 2), ring(block, 1)], axis=0)


def direct_scatter(groups, ring):
    rows = groups.shape[0] // 4
    own, plus, opposite, minus = (groups[i * rows:(i + 1) * rows] for i in range(4))
    return (
        own.astype(jnp.float32)
        + ring(plus, 1).astype(jnp.float32)
        + ring(opposite, 2).astype(jnp.float32)
        + ring(minus, -1).astype(jnp.float32)
    )


def shifted(value, axis, steps):
    count = lax.axis_size(axis)
    return lax.ppermute(value, axis, [(source, source + steps) for source in range(count - steps)])


def body(tokens, norm_gains, w_gate, w_up, w_down):
    section_count = lax.axis_size("section")
    split = section_count // LAYERS
    bit_count = split.bit_length() - 1
    position = lax.axis_index("section")
    section_layer = position // split
    member = position % split
    core = member % 2
    xpos = member // 2
    x_count = split // 2

    tp_count = lax.axis_size("tp")
    inner = 4
    outer = tp_count // inner

    def inner_ring(value, step):
        return tp_ring(value, inner, outer, "inner", step)

    def outer_ring(value, step):
        return tp_ring(value, inner, outer, "outer", step)

    micro_count, tok_dev, model_width = tokens.shape
    piece_width = model_width // split
    half_width = model_width // 2
    row_count = micro_count * tok_dev

    def pick(value, axis, which):
        shape = value.shape
        grouped = value.reshape(shape[:axis] + (x_count, 2, piece_width) + shape[axis + 1:])
        chosen = lax.dynamic_index_in_dim(grouped, which, axis + 1, keepdims=False)
        return chosen.reshape(shape[:axis] + (half_width,) + shape[axis + 1:])

    other = 1 - core
    gate_own = pick(w_gate[0], 0, core)
    gate_other = pick(w_gate[0], 0, other)
    up_own = pick(w_up[0], 0, core)
    up_other = pick(w_up[0], 0, other)
    down_own = pick(w_down[0], 1, core)
    down_other = pick(w_down[0], 1, other)
    norm_gain = lax.dynamic_index_in_dim(norm_gains, section_layer, 0, keepdims=False)
    gain_own = pick(norm_gain, 0, core)

    def from_tokens():
        rows = tokens.reshape(row_count, model_width).astype(jnp.float32)
        return pick(rows, 1, core), jnp.sum(rows * rows, axis=1, keepdims=True)

    def from_received(received):
        current = received.astype(jnp.float32)
        own_sq = jnp.sum(current * current, axis=1, keepdims=True)
        return current, own_sq + swapped(own_sq, "section", 1)

    def tick(current, square_sum):
        inv_rms = lax.rsqrt(square_sum / model_width + epsilon)
        normed = (current * inv_rms * gain_own).astype(jnp.bfloat16)
        gathered = ring_gather(direct_gather(normed, inner_ring), outer_ring)
        gathered_other = swapped(gathered, "section", 1)
        gate_proj = jnp.dot(gathered, gate_own, preferred_element_type=jnp.float32) + jnp.dot(
            gathered_other, gate_other, preferred_element_type=jnp.float32
        )
        up_proj = jnp.dot(gathered, up_own, preferred_element_type=jnp.float32) + jnp.dot(
            gathered_other, up_other, preferred_element_type=jnp.float32
        )
        active = (jax.nn.silu(gate_proj) * up_proj).astype(jnp.bfloat16)
        part_other = jnp.dot(active, down_other, preferred_element_type=jnp.float32).astype(jnp.bfloat16)
        part_from_other = swapped(part_other, "section", 1)
        part_own = jnp.dot(active, down_own, preferred_element_type=jnp.float32).astype(jnp.bfloat16)
        pair = (part_own.astype(jnp.float32) + part_from_other.astype(jnp.float32)).astype(jnp.bfloat16)
        summed = direct_scatter(ring_scatter(pair, outer_ring).astype(jnp.bfloat16), inner_ring).astype(jnp.bfloat16)
        summed = summed.astype(jnp.float32) + sum(
            swapped(summed, "section", 2 * mask).astype(jnp.float32) for mask in range(1, x_count)
        )
        full_half = (current + summed.astype(jnp.float32)).astype(jnp.bfloat16)
        block = lax.dynamic_index_in_dim(
            full_half.reshape(row_count, x_count, piece_width), xpos, 1, keepdims=False
        )
        return full_half, block

    blocks = []
    received = None
    for tick_index in range(LAYERS):
        if tick_index == 0:
            current, square_sum = from_tokens()
        else:
            current, square_sum = from_received(received)
        full_half, block = tick(current, square_sum)
        blocks.append(block)
        if tick_index < LAYERS - 1:
            received = shifted(full_half, "section", split)

    stacked = jnp.stack(blocks, axis=0)
    mine = lax.dynamic_index_in_dim(stacked, section_layer, 0, keepdims=False)
    return mine.reshape(1, micro_count, tok_dev, piece_width)


def solution(mesh):
    in_specs = (
        P(None, "tp", None),
        P(),
        P("section", None, "tp"),
        P("section", None, "tp"),
        P("section", "tp", None),
    )
    out_specs = P("section", None, "tp", None)
    return jax.shard_map(body, mesh=mesh, in_specs=in_specs, out_specs=out_specs, check_vma=False)
```

```python
import jax
import jax.numpy as jnp
from jax import lax
from jax.sharding import PartitionSpec as P

LAYERS = 2


epsilon = 1e-05


def permuted(value, sources, mapping):
    tp_count = lax.axis_size("tp")
    pairs = []
    for section, tp in sources:
        to_section, to_tp = mapping(section, tp)
        pairs.append((section * tp_count + tp, to_section * tp_count + to_tp))
    return lax.ppermute(value, ("section", "tp"), pairs)


def ring_gather(block, ring):
    half = block.shape[1] // 2
    from_left = ring(block, 1)
    from_right = ring(block, -1)
    opposite = jnp.concatenate(
        [ring(from_left[:, :half], 1), ring(from_right[:, half:], -1)], axis=1
    )
    return jnp.concatenate([block, from_right, opposite, from_left], axis=0)


def ring_scatter(groups, ring):
    rows = groups.shape[0] // 4
    half = groups.shape[1] // 2
    own, plus, opposite, minus = (groups[i * rows:(i + 1) * rows] for i in range(4))
    early_left = ring(opposite[:, :half], 1).astype(jnp.float32)
    early_right = ring(opposite[:, half:], -1).astype(jnp.float32)
    to_right = jnp.concatenate(
        [(plus[:, :half].astype(jnp.float32) + early_left).astype(jnp.bfloat16), plus[:, half:]], axis=1
    )
    to_left = jnp.concatenate(
        [minus[:, :half], (minus[:, half:].astype(jnp.float32) + early_right).astype(jnp.bfloat16)], axis=1
    )
    return (
        own.astype(jnp.float32)
        + ring(to_right, 1).astype(jnp.float32)
        + ring(to_left, -1).astype(jnp.float32)
    )


def direct_gather(block, ring):
    return jnp.concatenate([block, ring(block, -1), ring(block, 2), ring(block, 1)], axis=0)


def direct_scatter(groups, ring):
    rows = groups.shape[0] // 4
    own, plus, opposite, minus = (groups[i * rows:(i + 1) * rows] for i in range(4))
    return (
        own.astype(jnp.float32)
        + ring(plus, 1).astype(jnp.float32)
        + ring(opposite, 2).astype(jnp.float32)
        + ring(minus, -1).astype(jnp.float32)
    )


def body(tokens, norm_gains, w_gate, w_up, w_down):
    section_count = lax.axis_size("section")
    split = section_count // LAYERS
    bit_count = split.bit_length() - 1
    position = lax.axis_index("section")
    section_layer = position // split
    member = position % split
    core = member % 2
    xpos = member // 2
    x_count = split // 2

    tp_count = lax.axis_size("tp")
    inner = 4
    outer = tp_count // inner

    def group(layer):
        return [(s, t) for s in range(layer * split, (layer + 1) * split) for t in range(tp_count)]

    def inner_ring(layer):
        def ring(value, step):
            return permuted(
                value, group(layer), lambda s, t: (s, (t // inner) * inner + (t % inner + step) % inner)
            )
        return ring

    def outer_ring(layer):
        def ring(value, step):
            return permuted(
                value, group(layer), lambda s, t: (s, ((t // inner + step) % outer) * inner + t % inner)
            )
        return ring

    def swapped(value, layer, mask):
        return permuted(value, group(layer), lambda s, t: (s ^ mask, t))

    def forwarded(value, layer):
        return permuted(value, group(layer), lambda s, t: (s + split, t))

    micro_count, tok_dev, model_width = tokens.shape
    piece_width = model_width // split
    half_width = model_width // 2
    row_count = micro_count * tok_dev

    def pick(value, axis, which):
        shape = value.shape
        grouped = value.reshape(shape[:axis] + (x_count, 2, piece_width) + shape[axis + 1:])
        chosen = lax.dynamic_index_in_dim(grouped, which, axis + 1, keepdims=False)
        return chosen.reshape(shape[:axis] + (half_width,) + shape[axis + 1:])

    other = 1 - core
    gate_own = pick(w_gate[0], 0, core)
    gate_other = pick(w_gate[0], 0, other)
    up_own = pick(w_up[0], 0, core)
    up_other = pick(w_up[0], 0, other)
    down_own = pick(w_down[0], 1, core)
    down_other = pick(w_down[0], 1, other)
    norm_gain = lax.dynamic_index_in_dim(norm_gains, section_layer, 0, keepdims=False)
    gain_own = pick(norm_gain, 0, core)

    def from_tokens():
        rows = tokens.reshape(row_count, model_width).astype(jnp.float32)
        return pick(rows, 1, core), jnp.sum(rows * rows, axis=1, keepdims=True)

    def from_received(received, layer):
        current = received.astype(jnp.float32)
        own_sq = jnp.sum(current * current, axis=1, keepdims=True)
        return current, own_sq + swapped(own_sq, layer, 1)

    def tick(current, square_sum, layer):
        inv_rms = lax.rsqrt(square_sum / model_width + epsilon)
        normed = (current * inv_rms * gain_own).astype(jnp.bfloat16)
        gathered = ring_gather(ring_gather(normed, inner_ring(layer)), outer_ring(layer))
        gathered_other = swapped(gathered, layer, 1)
        gate_proj = jnp.dot(gathered, gate_own, preferred_element_type=jnp.float32) + jnp.dot(
            gathered_other, gate_other, preferred_element_type=jnp.float32
        )
        up_proj = jnp.dot(gathered, up_own, preferred_element_type=jnp.float32) + jnp.dot(
            gathered_other, up_other, preferred_element_type=jnp.float32
        )
        active = (jax.nn.silu(gate_proj) * up_proj).astype(jnp.bfloat16)
        part_other = jnp.dot(active, down_other, preferred_element_type=jnp.float32).astype(jnp.bfloat16)
        part_from_other = swapped(part_other, layer, 1)
        part_own = jnp.dot(active, down_own, preferred_element_type=jnp.float32).astype(jnp.bfloat16)
        pair = (part_own.astype(jnp.float32) + part_from_other.astype(jnp.float32)).astype(jnp.bfloat16)
        summed = ring_scatter(
            ring_scatter(pair, outer_ring(layer)).astype(jnp.bfloat16), inner_ring(layer)
        ).astype(jnp.bfloat16)
        summed = summed.astype(jnp.float32) + sum(
            swapped(summed, layer, 2 * mask).astype(jnp.float32) for mask in range(1, x_count)
        )
        full_half = (current + summed.astype(jnp.float32)).astype(jnp.bfloat16)
        block = lax.dynamic_index_in_dim(
            full_half.reshape(row_count, x_count, piece_width), xpos, 1, keepdims=False
        )
        return full_half, block

    blocks = []
    received = None
    for tick_index in range(LAYERS):
        if tick_index == 0:
            current, square_sum = from_tokens()
        else:
            current, square_sum = from_received(received, tick_index)
        full_half, block = tick(current, square_sum, tick_index)
        blocks.append(block)
        if tick_index < LAYERS - 1:
            received = forwarded(full_half, tick_index)

    stacked = jnp.stack(blocks, axis=0)
    mine = lax.dynamic_index_in_dim(stacked, section_layer, 0, keepdims=False)
    return mine.reshape(1, micro_count, tok_dev, piece_width)


def solution(mesh):
    in_specs = (
        P(None, "tp", None),
        P(),
        P("section", None, "tp"),
        P("section", None, "tp"),
        P("section", "tp", None),
    )
    out_specs = P("section", None, "tp", None)
    return jax.shard_map(body, mesh=mesh, in_specs=in_specs, out_specs=out_specs, check_vma=False)
```

```python
import jax
import jax.numpy as jnp
from jax import lax
from jax.sharding import PartitionSpec as P

LAYERS = 2
PIECES = 1


epsilon = 1e-05


def swapped(value, axis, mask):
    pairs = [(source, source ^ mask) for source in range(lax.axis_size(axis))]
    return lax.ppermute(value, axis, pairs)


def tp_ring(value, inner, outer, stage, step):
    pairs = []
    for source in range(inner * outer):
        high, low = divmod(source, inner)
        if stage == "inner":
            target = high * inner + (low + step) % inner
        else:
            target = ((high + step) % outer) * inner + low
        pairs.append((source, target))
    return lax.ppermute(value, "tp", pairs)


def ring_gather(block, ring):
    half = block.shape[1] // 2
    from_left = ring(block, 1)
    from_right = ring(block, -1)
    opposite = jnp.concatenate(
        [ring(from_left[:, :half], 1), ring(from_right[:, half:], -1)], axis=1
    )
    return jnp.concatenate([block, from_right, opposite, from_left], axis=0)


def ring_scatter(groups, ring):
    rows = groups.shape[0] // 4
    half = groups.shape[1] // 2
    own, plus, opposite, minus = (groups[i * rows:(i + 1) * rows] for i in range(4))
    early_left = ring(opposite[:, :half], 1).astype(jnp.float32)
    early_right = ring(opposite[:, half:], -1).astype(jnp.float32)
    to_right = jnp.concatenate(
        [(plus[:, :half].astype(jnp.float32) + early_left).astype(jnp.bfloat16), plus[:, half:]], axis=1
    )
    to_left = jnp.concatenate(
        [minus[:, :half], (minus[:, half:].astype(jnp.float32) + early_right).astype(jnp.bfloat16)], axis=1
    )
    return (
        own.astype(jnp.float32)
        + ring(to_right, 1).astype(jnp.float32)
        + ring(to_left, -1).astype(jnp.float32)
    )


def direct_gather(block, ring):
    return jnp.concatenate([block, ring(block, -1), ring(block, 2), ring(block, 1)], axis=0)


def direct_scatter(groups, ring):
    rows = groups.shape[0] // 4
    own, plus, opposite, minus = (groups[i * rows:(i + 1) * rows] for i in range(4))
    return (
        own.astype(jnp.float32)
        + ring(plus, 1).astype(jnp.float32)
        + ring(opposite, 2).astype(jnp.float32)
        + ring(minus, -1).astype(jnp.float32)
    )


def shifted(value, axis, steps):
    count = lax.axis_size(axis)
    return lax.ppermute(value, axis, [(source, source + steps) for source in range(count - steps)])


def body(tokens, norm_gains, w_gate, w_up, w_down):
    section_count = lax.axis_size("section")
    split = section_count // LAYERS
    bit_count = split.bit_length() - 1
    position = lax.axis_index("section")
    section_layer = position // split
    member = position % split
    core = member % 2
    xpos = member // 2
    x_count = split // 2

    tp_count = lax.axis_size("tp")
    inner = 4
    outer = tp_count // inner

    def inner_ring(value, step):
        return tp_ring(value, inner, outer, "inner", step)

    def outer_ring(value, step):
        return tp_ring(value, inner, outer, "outer", step)

    micro_count, tok_dev, model_width = tokens.shape
    piece_width = model_width // split
    half_width = model_width // 2
    row_count = tok_dev // PIECES
    piece_count = micro_count * PIECES
    tick_count = piece_count + LAYERS - 1

    def pick(value, axis, which):
        shape = value.shape
        grouped = value.reshape(shape[:axis] + (x_count, 2, piece_width) + shape[axis + 1:])
        chosen = lax.dynamic_index_in_dim(grouped, which, axis + 1, keepdims=False)
        return chosen.reshape(shape[:axis] + (half_width,) + shape[axis + 1:])

    other = 1 - core
    gate_own = pick(w_gate[0], 0, core)
    gate_other = pick(w_gate[0], 0, other)
    up_own = pick(w_up[0], 0, core)
    up_other = pick(w_up[0], 0, other)
    down_own = pick(w_down[0], 1, core)
    down_other = pick(w_down[0], 1, other)
    norm_gain = lax.dynamic_index_in_dim(norm_gains, section_layer, 0, keepdims=False)
    gain_own = pick(norm_gain, 0, core)

    def from_tokens(piece_index):
        micro_index, part = divmod(piece_index, PIECES)
        rows = tokens[micro_index, part * row_count:(part + 1) * row_count].astype(jnp.float32)
        return pick(rows, 1, core), jnp.sum(rows * rows, axis=1, keepdims=True)

    def from_received(partials, piece_index):
        base, _ = from_tokens(piece_index)
        total = base + sum(part.astype(jnp.float32) for part in partials)
        current = total.astype(jnp.bfloat16).astype(jnp.float32)
        own_sq = jnp.sum(current * current, axis=1, keepdims=True)
        return current, own_sq + swapped(own_sq, "section", 1)

    def tick(current, square_sum):
        inv_rms = lax.rsqrt(square_sum / model_width + epsilon)
        normed = (current * inv_rms * gain_own).astype(jnp.bfloat16)
        gathered = ring_gather(direct_gather(normed, inner_ring), outer_ring)
        gathered_other = swapped(gathered, "section", 1)
        gate_proj = jnp.dot(gathered, gate_own, preferred_element_type=jnp.float32) + jnp.dot(
            gathered_other, gate_other, preferred_element_type=jnp.float32
        )
        up_proj = jnp.dot(gathered, up_own, preferred_element_type=jnp.float32) + jnp.dot(
            gathered_other, up_other, preferred_element_type=jnp.float32
        )
        active = (jax.nn.silu(gate_proj) * up_proj).astype(jnp.bfloat16)
        part_other = jnp.dot(active, down_other, preferred_element_type=jnp.float32).astype(jnp.bfloat16)
        part_from_other = swapped(part_other, "section", 1)
        part_own = jnp.dot(active, down_own, preferred_element_type=jnp.float32).astype(jnp.bfloat16)
        pair = (part_own.astype(jnp.float32) + part_from_other.astype(jnp.float32)).astype(jnp.bfloat16)
        reduced = direct_scatter(ring_scatter(pair, outer_ring).astype(jnp.bfloat16), inner_ring).astype(jnp.bfloat16)
        pieces = reduced.reshape(row_count, x_count, piece_width)
        own_piece = lax.dynamic_index_in_dim(pieces, xpos, 1, keepdims=False).astype(jnp.float32)
        for mask in range(1, x_count):
            sent = lax.dynamic_index_in_dim(pieces, xpos ^ mask, 1, keepdims=False)
            own_piece = own_piece + swapped(sent, "section", 2 * mask).astype(jnp.float32)
        current_piece = lax.dynamic_index_in_dim(
            current.reshape(row_count, x_count, piece_width), xpos, 1, keepdims=False
        )
        block = (current_piece + own_piece).astype(jnp.bfloat16)
        return reduced, block

    blocks = []
    received = None
    for tick_index in range(tick_count):
        if tick_index == 0:
            current, square_sum = from_tokens(0)
        elif tick_index >= piece_count:
            current, square_sum = from_received(received, tick_index - 1)
        else:
            first_current, first_sum = from_tokens(tick_index)
            later_current, later_sum = from_received(received, tick_index - 1)
            is_first = section_layer == 0
            current = jnp.where(is_first, first_current, later_current)
            square_sum = jnp.where(is_first, first_sum, later_sum)
        reduced, block = tick(current, square_sum)
        blocks.append(block)
        if tick_index < tick_count - 1:
            received = [
                lax.ppermute(
                    reduced,
                    "section",
                    [(source, (source + split) ^ (2 * mask)) for source in range(section_count - split)],
                )
                for mask in range(x_count)
            ]

    stacked = jnp.stack(blocks, axis=0)
    outputs = []
    for micro_index in range(micro_count):
        parts = [
            lax.dynamic_index_in_dim(stacked, micro_index * PIECES + part + section_layer, 0, keepdims=False)
            for part in range(PIECES)
        ]
        outputs.append(jnp.concatenate(parts, axis=0))
    return jnp.stack(outputs, axis=0)[None]


def solution(mesh):
    in_specs = (
        P(None, "tp", None),
        P(),
        P("section", None, "tp"),
        P("section", None, "tp"),
        P("section", "tp", None),
    )
    out_specs = P("section", None, "tp", None)
    return jax.shard_map(body, mesh=mesh, in_specs=in_specs, out_specs=out_specs, check_vma=False)
```

```python
import jax
import jax.numpy as jnp
from jax import lax
from jax.sharding import PartitionSpec as P

LAYERS = 2
PIECES = 1


epsilon = 1e-05


def swapped(value, axis, mask):
    pairs = [(source, source ^ mask) for source in range(lax.axis_size(axis))]
    return lax.ppermute(value, axis, pairs)


def tp_ring(value, inner, outer, stage, step):
    pairs = []
    for source in range(inner * outer):
        high, low = divmod(source, inner)
        if stage == "inner":
            target = high * inner + (low + step) % inner
        else:
            target = ((high + step) % outer) * inner + low
        pairs.append((source, target))
    return lax.ppermute(value, "tp", pairs)


def ring_gather(block, ring):
    half = block.shape[1] // 2
    from_left = ring(block, 1)
    from_right = ring(block, -1)
    opposite = jnp.concatenate(
        [ring(from_left[:, :half], 1), ring(from_right[:, half:], -1)], axis=1
    )
    return jnp.concatenate([block, from_right, opposite, from_left], axis=0)


def ring_scatter(groups, ring):
    rows = groups.shape[0] // 4
    half = groups.shape[1] // 2
    own, plus, opposite, minus = (groups[i * rows:(i + 1) * rows] for i in range(4))
    early_left = ring(opposite[:, :half], 1).astype(jnp.float32)
    early_right = ring(opposite[:, half:], -1).astype(jnp.float32)
    to_right = jnp.concatenate(
        [(plus[:, :half].astype(jnp.float32) + early_left).astype(jnp.bfloat16), plus[:, half:]], axis=1
    )
    to_left = jnp.concatenate(
        [minus[:, :half], (minus[:, half:].astype(jnp.float32) + early_right).astype(jnp.bfloat16)], axis=1
    )
    return (
        own.astype(jnp.float32)
        + ring(to_right, 1).astype(jnp.float32)
        + ring(to_left, -1).astype(jnp.float32)
    )


def direct_gather(block, ring):
    return jnp.concatenate([block, ring(block, -1), ring(block, 2), ring(block, 1)], axis=0)


def direct_scatter(groups, ring):
    rows = groups.shape[0] // 4
    own, plus, opposite, minus = (groups[i * rows:(i + 1) * rows] for i in range(4))
    return (
        own.astype(jnp.float32)
        + ring(plus, 1).astype(jnp.float32)
        + ring(opposite, 2).astype(jnp.float32)
        + ring(minus, -1).astype(jnp.float32)
    )


def shifted(value, axis, steps):
    count = lax.axis_size(axis)
    return lax.ppermute(value, axis, [(source, source + steps) for source in range(count - steps)])


def body(tokens, norm_gains, w_gate, w_up, w_down):
    section_count = lax.axis_size("section")
    split = section_count // LAYERS
    bit_count = split.bit_length() - 1
    position = lax.axis_index("section")
    section_layer = position // split
    member = position % split
    core = member % 2
    xpos = member // 2
    x_count = split // 2

    tp_count = lax.axis_size("tp")
    inner = 4
    outer = tp_count // inner

    def inner_ring(value, step):
        return tp_ring(value, inner, outer, "inner", step)

    def outer_ring(value, step):
        return tp_ring(value, inner, outer, "outer", step)

    micro_count, tok_dev, model_width = tokens.shape
    piece_width = model_width // split
    half_width = model_width // 2
    row_count = tok_dev // PIECES
    piece_count = micro_count * PIECES
    tick_count = piece_count + LAYERS - 1

    def pick(value, axis, which):
        shape = value.shape
        grouped = value.reshape(shape[:axis] + (x_count, 2, piece_width) + shape[axis + 1:])
        chosen = lax.dynamic_index_in_dim(grouped, which, axis + 1, keepdims=False)
        return chosen.reshape(shape[:axis] + (half_width,) + shape[axis + 1:])

    other = 1 - core
    gate_own = pick(w_gate[0], 0, core)
    gate_other = pick(w_gate[0], 0, other)
    up_own = pick(w_up[0], 0, core)
    up_other = pick(w_up[0], 0, other)
    down_own = pick(w_down[0], 1, core)
    down_other = pick(w_down[0], 1, other)
    norm_gain = lax.dynamic_index_in_dim(norm_gains, section_layer, 0, keepdims=False)
    gain_own = pick(norm_gain, 0, core)

    def from_tokens(piece_index):
        micro_index, part = divmod(piece_index, PIECES)
        rows = tokens[micro_index, part * row_count:(part + 1) * row_count].astype(jnp.float32)
        return pick(rows, 1, core), jnp.sum(rows * rows, axis=1, keepdims=True)

    def from_received(partials, piece_index):
        base, _ = from_tokens(piece_index)
        total = base + sum(part.astype(jnp.float32) for part in partials)
        current = total.astype(jnp.bfloat16).astype(jnp.float32)
        own_sq = jnp.sum(current * current, axis=1, keepdims=True)
        return current, own_sq + swapped(own_sq, "section", 1)

    def tick(current, square_sum):
        inv_rms = lax.rsqrt(square_sum / model_width + epsilon)
        normed = (current * inv_rms * gain_own).astype(jnp.bfloat16)
        gathered = ring_gather(direct_gather(normed, inner_ring), outer_ring)
        gathered_other = swapped(gathered, "section", 1)
        gate_proj = jnp.dot(gathered, gate_own, preferred_element_type=jnp.float32) + jnp.dot(
            gathered_other, gate_other, preferred_element_type=jnp.float32
        )
        up_proj = jnp.dot(gathered, up_own, preferred_element_type=jnp.float32) + jnp.dot(
            gathered_other, up_other, preferred_element_type=jnp.float32
        )
        active = (jax.nn.silu(gate_proj) * up_proj).astype(jnp.bfloat16)
        part_other = jnp.dot(active, down_other, preferred_element_type=jnp.float32).astype(jnp.bfloat16)
        part_from_other = swapped(part_other, "section", 1)
        part_own = jnp.dot(active, down_own, preferred_element_type=jnp.float32).astype(jnp.bfloat16)
        pair = (part_own.astype(jnp.float32) + part_from_other.astype(jnp.float32)).astype(jnp.bfloat16)
        reduced = direct_scatter(ring_scatter(pair, outer_ring).astype(jnp.bfloat16), inner_ring).astype(jnp.bfloat16)
        current_piece = lax.dynamic_index_in_dim(
            current.reshape(row_count, x_count, piece_width), xpos, 1, keepdims=False
        )
        return reduced, current_piece

    blocks = []
    received = None
    for tick_index in range(tick_count):
        if tick_index == 0:
            current, square_sum = from_tokens(0)
        elif tick_index >= piece_count:
            current, square_sum = from_received(received, tick_index - 1)
        else:
            first_current, first_sum = from_tokens(tick_index)
            later_current, later_sum = from_received(received, tick_index - 1)
            is_first = section_layer == 0
            current = jnp.where(is_first, first_current, later_current)
            square_sum = jnp.where(is_first, first_sum, later_sum)
        reduced, current_piece = tick(current, square_sum)
        blocks.append((reduced, current_piece))
        if tick_index < tick_count - 1:
            received = [
                lax.ppermute(
                    reduced,
                    "section",
                    [(source, (source + split) ^ (2 * mask)) for source in range(section_count - split)],
                )
                for mask in range(x_count)
            ]

    reduced_all = jnp.stack([reduced for reduced, _ in blocks], axis=0)
    current_all = jnp.stack([piece for _, piece in blocks], axis=0)
    mine = lax.dynamic_slice_in_dim(reduced_all, section_layer, piece_count, 0)
    pieces = mine.reshape(piece_count, row_count, x_count, piece_width)
    total = lax.dynamic_index_in_dim(pieces, xpos, 2, keepdims=False).astype(jnp.float32)
    for mask in range(1, x_count):
        sent = lax.dynamic_index_in_dim(pieces, xpos ^ mask, 2, keepdims=False)
        total = total + swapped(sent, "section", 2 * mask).astype(jnp.float32)
    base = lax.dynamic_slice_in_dim(current_all, section_layer, piece_count, 0)
    result = (base + total).astype(jnp.bfloat16)
    return result.reshape(1, micro_count, tok_dev, piece_width)


def solution(mesh):
    in_specs = (
        P(None, "tp", None),
        P(),
        P("section", None, "tp"),
        P("section", None, "tp"),
        P("section", "tp", None),
    )
    out_specs = P("section", None, "tp", None)
    return jax.shard_map(body, mesh=mesh, in_specs=in_specs, out_specs=out_specs, check_vma=False)
```

```python
import jax
import jax.numpy as jnp
from jax import lax
from jax.sharding import PartitionSpec as P

LAYERS = 2
PIECES = 2


epsilon = 1e-05


def swapped(value, axis, mask):
    pairs = [(source, source ^ mask) for source in range(lax.axis_size(axis))]
    return lax.ppermute(value, axis, pairs)


def tp_ring(value, inner, outer, stage, step):
    pairs = []
    for source in range(inner * outer):
        high, low = divmod(source, inner)
        if stage == "inner":
            target = high * inner + (low + step) % inner
        else:
            target = ((high + step) % outer) * inner + low
        pairs.append((source, target))
    return lax.ppermute(value, "tp", pairs)


def ring_gather(block, ring):
    half = block.shape[1] // 2
    from_left = ring(block, 1)
    from_right = ring(block, -1)
    opposite = jnp.concatenate(
        [ring(from_left[:, :half], 1), ring(from_right[:, half:], -1)], axis=1
    )
    return jnp.concatenate([block, from_right, opposite, from_left], axis=0)


def ring_scatter(groups, ring):
    rows = groups.shape[0] // 4
    half = groups.shape[1] // 2
    own, plus, opposite, minus = (groups[i * rows:(i + 1) * rows] for i in range(4))
    early_left = ring(opposite[:, :half], 1).astype(jnp.float32)
    early_right = ring(opposite[:, half:], -1).astype(jnp.float32)
    to_right = jnp.concatenate(
        [(plus[:, :half].astype(jnp.float32) + early_left).astype(jnp.bfloat16), plus[:, half:]], axis=1
    )
    to_left = jnp.concatenate(
        [minus[:, :half], (minus[:, half:].astype(jnp.float32) + early_right).astype(jnp.bfloat16)], axis=1
    )
    return (
        own.astype(jnp.float32)
        + ring(to_right, 1).astype(jnp.float32)
        + ring(to_left, -1).astype(jnp.float32)
    )


def direct_gather(block, ring):
    return jnp.concatenate([block, ring(block, -1), ring(block, 2), ring(block, 1)], axis=0)


def direct_scatter(groups, ring):
    rows = groups.shape[0] // 4
    own, plus, opposite, minus = (groups[i * rows:(i + 1) * rows] for i in range(4))
    return (
        own.astype(jnp.float32)
        + ring(plus, 1).astype(jnp.float32)
        + ring(opposite, 2).astype(jnp.float32)
        + ring(minus, -1).astype(jnp.float32)
    )


def shifted(value, axis, steps):
    count = lax.axis_size(axis)
    return lax.ppermute(value, axis, [(source, source + steps) for source in range(count - steps)])


def body(tokens, norm_gains, w_gate, w_up, w_down):
    section_count = lax.axis_size("section")
    split = section_count // LAYERS
    bit_count = split.bit_length() - 1
    position = lax.axis_index("section")
    section_layer = position // split
    member = position % split
    core = member % 2
    xpos = member // 2
    x_count = split // 2

    tp_count = lax.axis_size("tp")
    inner = 4
    outer = tp_count // inner

    def inner_ring(value, step):
        return tp_ring(value, inner, outer, "inner", step)

    def outer_ring(value, step):
        return tp_ring(value, inner, outer, "outer", step)

    micro_count, tok_dev, model_width = tokens.shape
    piece_width = model_width // split
    half_width = model_width // 2
    row_count = tok_dev // PIECES
    piece_count = micro_count * PIECES
    tick_count = piece_count + LAYERS - 1

    def pick(value, axis, which):
        shape = value.shape
        grouped = value.reshape(shape[:axis] + (x_count, 2, piece_width) + shape[axis + 1:])
        chosen = lax.dynamic_index_in_dim(grouped, which, axis + 1, keepdims=False)
        return chosen.reshape(shape[:axis] + (half_width,) + shape[axis + 1:])

    other = 1 - core
    gate_own = pick(w_gate[0], 0, core)
    gate_other = pick(w_gate[0], 0, other)
    up_own = pick(w_up[0], 0, core)
    up_other = pick(w_up[0], 0, other)
    down_own = pick(w_down[0], 1, core)
    down_other = pick(w_down[0], 1, other)
    norm_gain = lax.dynamic_index_in_dim(norm_gains, section_layer, 0, keepdims=False)
    gain_own = pick(norm_gain, 0, core)

    def from_tokens(piece_index):
        micro_index, part = divmod(piece_index, PIECES)
        rows = tokens[micro_index, part * row_count:(part + 1) * row_count].astype(jnp.float32)
        return pick(rows, 1, core), jnp.sum(rows * rows, axis=1, keepdims=True)

    def from_received(received):
        current = received.astype(jnp.float32)
        own_sq = jnp.sum(current * current, axis=1, keepdims=True)
        return current, own_sq + swapped(own_sq, "section", 1)

    def tick(current, square_sum):
        inv_rms = lax.rsqrt(square_sum / model_width + epsilon)
        normed = (current * inv_rms * gain_own).astype(jnp.bfloat16)
        gathered = ring_gather(direct_gather(normed, inner_ring), outer_ring)
        gathered_other = swapped(gathered, "section", 1)
        gate_proj = jnp.dot(gathered, gate_own, preferred_element_type=jnp.float32) + jnp.dot(
            gathered_other, gate_other, preferred_element_type=jnp.float32
        )
        up_proj = jnp.dot(gathered, up_own, preferred_element_type=jnp.float32) + jnp.dot(
            gathered_other, up_other, preferred_element_type=jnp.float32
        )
        active = (jax.nn.silu(gate_proj) * up_proj).astype(jnp.bfloat16)
        part_other = jnp.dot(active, down_other, preferred_element_type=jnp.float32).astype(jnp.bfloat16)
        part_from_other = swapped(part_other, "section", 1)
        part_own = jnp.dot(active, down_own, preferred_element_type=jnp.float32).astype(jnp.bfloat16)
        pair = (part_own.astype(jnp.float32) + part_from_other.astype(jnp.float32)).astype(jnp.bfloat16)
        summed = direct_scatter(ring_scatter(pair, outer_ring).astype(jnp.bfloat16), inner_ring).astype(jnp.bfloat16)
        summed = summed.astype(jnp.float32) + sum(
            swapped(summed, "section", 2 * mask).astype(jnp.float32) for mask in range(1, x_count)
        )
        full_half = (current + summed.astype(jnp.float32)).astype(jnp.bfloat16)
        block = lax.dynamic_index_in_dim(
            full_half.reshape(row_count, x_count, piece_width), xpos, 1, keepdims=False
        )
        return full_half, block

    blocks = []
    received = None
    for tick_index in range(tick_count):
        if tick_index == 0:
            current, square_sum = from_tokens(0)
        elif tick_index >= piece_count:
            current, square_sum = from_received(received)
        else:
            first_current, first_sum = from_tokens(tick_index)
            later_current, later_sum = from_received(received)
            is_first = section_layer == 0
            current = jnp.where(is_first, first_current, later_current)
            square_sum = jnp.where(is_first, first_sum, later_sum)
        full_half, block = tick(current, square_sum)
        blocks.append(block)
        if tick_index < tick_count - 1:
            received = shifted(full_half, "section", split)

    stacked = jnp.stack(blocks, axis=0)
    outputs = []
    for micro_index in range(micro_count):
        parts = [
            lax.dynamic_index_in_dim(stacked, micro_index * PIECES + part + section_layer, 0, keepdims=False)
            for part in range(PIECES)
        ]
        outputs.append(jnp.concatenate(parts, axis=0))
    return jnp.stack(outputs, axis=0)[None]


def solution(mesh):
    in_specs = (
        P(None, "tp", None),
        P(),
        P("section", None, "tp"),
        P("section", None, "tp"),
        P("section", "tp", None),
    )
    out_specs = P("section", None, "tp", None)
    return jax.shard_map(body, mesh=mesh, in_specs=in_specs, out_specs=out_specs, check_vma=False)
```

```python
import jax
import jax.numpy as jnp
from jax import lax
from jax.sharding import PartitionSpec as P

LAYERS = 2
PIECES = 1


epsilon = 1e-05


def swapped(value, axis, mask):
    pairs = [(source, source ^ mask) for source in range(lax.axis_size(axis))]
    return lax.ppermute(value, axis, pairs)


def tp_ring(value, inner, outer, stage, step):
    pairs = []
    for source in range(inner * outer):
        high, low = divmod(source, inner)
        if stage == "inner":
            target = high * inner + (low + step) % inner
        else:
            target = ((high + step) % outer) * inner + low
        pairs.append((source, target))
    return lax.ppermute(value, "tp", pairs)


def ring_gather(block, ring):
    half = block.shape[1] // 2
    from_left = ring(block, 1)
    from_right = ring(block, -1)
    opposite = jnp.concatenate(
        [ring(from_left[:, :half], 1), ring(from_right[:, half:], -1)], axis=1
    )
    return jnp.concatenate([block, from_right, opposite, from_left], axis=0)


def ring_scatter(groups, ring):
    rows = groups.shape[0] // 4
    half = groups.shape[1] // 2
    own, plus, opposite, minus = (groups[i * rows:(i + 1) * rows] for i in range(4))
    early_left = ring(opposite[:, :half], 1).astype(jnp.float32)
    early_right = ring(opposite[:, half:], -1).astype(jnp.float32)
    to_right = jnp.concatenate(
        [(plus[:, :half].astype(jnp.float32) + early_left).astype(jnp.bfloat16), plus[:, half:]], axis=1
    )
    to_left = jnp.concatenate(
        [minus[:, :half], (minus[:, half:].astype(jnp.float32) + early_right).astype(jnp.bfloat16)], axis=1
    )
    return (
        own.astype(jnp.float32)
        + ring(to_right, 1).astype(jnp.float32)
        + ring(to_left, -1).astype(jnp.float32)
    )


def direct_gather(block, ring):
    return jnp.concatenate([block, ring(block, -1), ring(block, 2), ring(block, 1)], axis=0)


def direct_scatter(groups, ring):
    rows = groups.shape[0] // 4
    own, plus, opposite, minus = (groups[i * rows:(i + 1) * rows] for i in range(4))
    return (
        own.astype(jnp.float32)
        + ring(plus, 1).astype(jnp.float32)
        + ring(opposite, 2).astype(jnp.float32)
        + ring(minus, -1).astype(jnp.float32)
    )


def shifted(value, axis, steps):
    count = lax.axis_size(axis)
    return lax.ppermute(value, axis, [(source, source + steps) for source in range(count - steps)])


def body(tokens, norm_gains, w_gate, w_up, w_down):
    section_count = lax.axis_size("section")
    split = section_count // LAYERS
    bit_count = split.bit_length() - 1
    position = lax.axis_index("section")
    section_layer = position // split
    member = position % split
    core = member % 2
    xpos = member // 2
    x_count = split // 2

    tp_count = lax.axis_size("tp")
    inner = 4
    outer = tp_count // inner

    def inner_ring(value, step):
        return tp_ring(value, inner, outer, "inner", step)

    def outer_ring(value, step):
        return tp_ring(value, inner, outer, "outer", step)

    micro_count, tok_dev, model_width = tokens.shape
    piece_width = model_width // split
    half_width = model_width // 2
    row_count = tok_dev // PIECES
    piece_count = micro_count * PIECES
    tick_count = piece_count + LAYERS - 1

    def pick(value, axis, which):
        shape = value.shape
        grouped = value.reshape(shape[:axis] + (x_count, 2, piece_width) + shape[axis + 1:])
        chosen = lax.dynamic_index_in_dim(grouped, which, axis + 1, keepdims=False)
        return chosen.reshape(shape[:axis] + (half_width,) + shape[axis + 1:])

    other = 1 - core
    gate_own = pick(w_gate[0], 0, core)
    gate_other = pick(w_gate[0], 0, other)
    up_own = pick(w_up[0], 0, core)
    up_other = pick(w_up[0], 0, other)
    down_own = pick(w_down[0], 1, core)
    down_other = pick(w_down[0], 1, other)
    gate_both = jnp.concatenate([gate_own, swapped(gate_other, "section", 1)], axis=1)
    up_both = jnp.concatenate([up_own, swapped(up_other, "section", 1)], axis=1)
    down_theirs = swapped(down_other, "section", 1)
    unit_count = gate_own.shape[1]
    norm_gain = lax.dynamic_index_in_dim(norm_gains, section_layer, 0, keepdims=False)
    gain_own = pick(norm_gain, 0, core)

    def from_tokens(piece_index):
        micro_index, part = divmod(piece_index, PIECES)
        rows = tokens[micro_index, part * row_count:(part + 1) * row_count].astype(jnp.float32)
        return pick(rows, 1, core), jnp.sum(rows * rows, axis=1, keepdims=True)

    def from_received(received):
        current = received.astype(jnp.float32)
        own_sq = jnp.sum(current * current, axis=1, keepdims=True)
        return current, own_sq + swapped(own_sq, "section", 1)

    def tick(current, square_sum):
        inv_rms = lax.rsqrt(square_sum / model_width + epsilon)
        normed = (current * inv_rms * gain_own).astype(jnp.bfloat16)
        gathered = ring_gather(direct_gather(normed, inner_ring), outer_ring)
        gate_terms = jnp.dot(gathered, gate_both, preferred_element_type=jnp.float32)
        up_terms = jnp.dot(gathered, up_both, preferred_element_type=jnp.float32)
        terms_from_other = swapped(
            jnp.concatenate([gate_terms[:, unit_count:], up_terms[:, unit_count:]], axis=1), "section", 1
        )
        gate_proj = gate_terms[:, :unit_count] + terms_from_other[:, :unit_count]
        up_proj = up_terms[:, :unit_count] + terms_from_other[:, unit_count:]
        active = (jax.nn.silu(gate_proj) * up_proj).astype(jnp.bfloat16)
        active_from_other = swapped(active, "section", 1)
        part_own = jnp.dot(active, down_own, preferred_element_type=jnp.float32).astype(jnp.bfloat16)
        part_from_other = jnp.dot(
            active_from_other, down_theirs, preferred_element_type=jnp.float32
        ).astype(jnp.bfloat16)
        pair = (part_own.astype(jnp.float32) + part_from_other.astype(jnp.float32)).astype(jnp.bfloat16)
        summed = direct_scatter(ring_scatter(pair, outer_ring).astype(jnp.bfloat16), inner_ring).astype(jnp.bfloat16)
        summed = summed.astype(jnp.float32) + sum(
            swapped(summed, "section", 2 * mask).astype(jnp.float32) for mask in range(1, x_count)
        )
        full_half = (current + summed.astype(jnp.float32)).astype(jnp.bfloat16)
        block = lax.dynamic_index_in_dim(
            full_half.reshape(row_count, x_count, piece_width), xpos, 1, keepdims=False
        )
        return full_half, block

    blocks = []
    received = None
    for tick_index in range(tick_count):
        if tick_index == 0:
            current, square_sum = from_tokens(0)
        elif tick_index >= piece_count:
            current, square_sum = from_received(received)
        else:
            first_current, first_sum = from_tokens(tick_index)
            later_current, later_sum = from_received(received)
            is_first = section_layer == 0
            current = jnp.where(is_first, first_current, later_current)
            square_sum = jnp.where(is_first, first_sum, later_sum)
        full_half, block = tick(current, square_sum)
        blocks.append(block)
        if tick_index < tick_count - 1:
            received = shifted(full_half, "section", split)

    stacked = jnp.stack(blocks, axis=0)
    outputs = []
    for micro_index in range(micro_count):
        parts = [
            lax.dynamic_index_in_dim(stacked, micro_index * PIECES + part + section_layer, 0, keepdims=False)
            for part in range(PIECES)
        ]
        outputs.append(jnp.concatenate(parts, axis=0))
    return jnp.stack(outputs, axis=0)[None]


def solution(mesh):
    in_specs = (
        P(None, "tp", None),
        P(),
        P("section", None, "tp"),
        P("section", None, "tp"),
        P("section", "tp", None),
    )
    out_specs = P("section", None, "tp", None)
    return jax.shard_map(body, mesh=mesh, in_specs=in_specs, out_specs=out_specs, check_vma=False)
```

```python
import jax
import jax.numpy as jnp
from jax import lax
from jax.sharding import PartitionSpec as P

LAYERS = 2
PIECES = 1


epsilon = 1e-05


def swapped(value, axis, mask):
    pairs = [(source, source ^ mask) for source in range(lax.axis_size(axis))]
    return lax.ppermute(value, axis, pairs)


def tp_ring(value, inner, outer, stage, step):
    pairs = []
    for source in range(inner * outer):
        high, low = divmod(source, inner)
        if stage == "inner":
            target = high * inner + (low + step) % inner
        else:
            target = ((high + step) % outer) * inner + low
        pairs.append((source, target))
    return lax.ppermute(value, "tp", pairs)


def ring_gather(block, ring):
    half = block.shape[1] // 2
    from_left = ring(block, 1)
    from_right = ring(block, -1)
    opposite = jnp.concatenate(
        [ring(from_left[:, :half], 1), ring(from_right[:, half:], -1)], axis=1
    )
    return jnp.concatenate([block, from_right, opposite, from_left], axis=0)


def ring_scatter(groups, ring):
    rows = groups.shape[0] // 4
    half = groups.shape[1] // 2
    own, plus, opposite, minus = (groups[i * rows:(i + 1) * rows] for i in range(4))
    early_left = ring(opposite[:, :half], 1).astype(jnp.float32)
    early_right = ring(opposite[:, half:], -1).astype(jnp.float32)
    to_right = jnp.concatenate(
        [(plus[:, :half].astype(jnp.float32) + early_left).astype(jnp.bfloat16), plus[:, half:]], axis=1
    )
    to_left = jnp.concatenate(
        [minus[:, :half], (minus[:, half:].astype(jnp.float32) + early_right).astype(jnp.bfloat16)], axis=1
    )
    return (
        own.astype(jnp.float32)
        + ring(to_right, 1).astype(jnp.float32)
        + ring(to_left, -1).astype(jnp.float32)
    )


def direct_gather(block, ring):
    return jnp.concatenate([block, ring(block, -1), ring(block, 2), ring(block, 1)], axis=0)


def direct_scatter(groups, ring):
    rows = groups.shape[0] // 4
    own, plus, opposite, minus = (groups[i * rows:(i + 1) * rows] for i in range(4))
    return (
        own.astype(jnp.float32)
        + ring(plus, 1).astype(jnp.float32)
        + ring(opposite, 2).astype(jnp.float32)
        + ring(minus, -1).astype(jnp.float32)
    )


def shifted(value, axis, steps):
    count = lax.axis_size(axis)
    return lax.ppermute(value, axis, [(source, source + steps) for source in range(count - steps)])


def body(tokens, norm_gains, w_gate, w_up, w_down):
    section_count = lax.axis_size("section")
    split = section_count // LAYERS
    bit_count = split.bit_length() - 1
    position = lax.axis_index("section")
    section_layer = position // split
    member = position % split
    core = member % 2
    xpos = member // 2
    x_count = split // 2

    tp_count = lax.axis_size("tp")
    inner = 4
    outer = tp_count // inner

    def inner_ring_for(layers):
        def ring(value, step):
            pairs = []
            for section in range(section_count):
                if section // split not in layers:
                    continue
                for source in range(tp_count):
                    high, low = divmod(source, inner)
                    target = high * inner + (low + step) % inner
                    pairs.append((section * tp_count + source, section * tp_count + target))
            return lax.ppermute(value, ("section", "tp"), pairs)
        return ring

    def outer_ring(value, step):
        return tp_ring(value, inner, outer, "outer", step)

    micro_count, tok_dev, model_width = tokens.shape
    piece_width = model_width // split
    half_width = model_width // 2
    row_count = tok_dev // PIECES
    piece_count = micro_count * PIECES
    tick_count = piece_count + LAYERS - 1

    def pick(value, axis, which):
        shape = value.shape
        grouped = value.reshape(shape[:axis] + (x_count, 2, piece_width) + shape[axis + 1:])
        chosen = lax.dynamic_index_in_dim(grouped, which, axis + 1, keepdims=False)
        return chosen.reshape(shape[:axis] + (half_width,) + shape[axis + 1:])

    other = 1 - core
    gate_own = pick(w_gate[0], 0, core)
    gate_other = pick(w_gate[0], 0, other)
    up_own = pick(w_up[0], 0, core)
    up_other = pick(w_up[0], 0, other)
    down_own = pick(w_down[0], 1, core)
    down_other = pick(w_down[0], 1, other)
    gate_both = jnp.concatenate([gate_own, swapped(gate_other, "section", 1)], axis=1)
    up_both = jnp.concatenate([up_own, swapped(up_other, "section", 1)], axis=1)
    down_theirs = swapped(down_other, "section", 1)
    unit_count = gate_own.shape[1]
    norm_gain = lax.dynamic_index_in_dim(norm_gains, section_layer, 0, keepdims=False)
    gain_own = pick(norm_gain, 0, core)

    def from_tokens(piece_index):
        micro_index, part = divmod(piece_index, PIECES)
        rows = tokens[micro_index, part * row_count:(part + 1) * row_count].astype(jnp.float32)
        return pick(rows, 1, core), jnp.sum(rows * rows, axis=1, keepdims=True)

    def from_received(received):
        current = received.astype(jnp.float32)
        own_sq = jnp.sum(current * current, axis=1, keepdims=True)
        return current, own_sq + swapped(own_sq, "section", 1)

    def tick(current, square_sum, layers):
        inner_ring = inner_ring_for(layers)
        inv_rms = lax.rsqrt(square_sum / model_width + epsilon)
        normed = (current * inv_rms * gain_own).astype(jnp.bfloat16)
        gathered = ring_gather(direct_gather(normed, inner_ring), outer_ring)
        gate_terms = jnp.dot(gathered, gate_both, preferred_element_type=jnp.float32)
        up_terms = jnp.dot(gathered, up_both, preferred_element_type=jnp.float32)
        terms_from_other = swapped(
            jnp.concatenate([gate_terms[:, unit_count:], up_terms[:, unit_count:]], axis=1), "section", 1
        )
        gate_proj = gate_terms[:, :unit_count] + terms_from_other[:, :unit_count]
        up_proj = up_terms[:, :unit_count] + terms_from_other[:, unit_count:]
        active = (jax.nn.silu(gate_proj) * up_proj).astype(jnp.bfloat16)
        active_from_other = swapped(active, "section", 1)
        part_own = jnp.dot(active, down_own, preferred_element_type=jnp.float32).astype(jnp.bfloat16)
        part_from_other = jnp.dot(
            active_from_other, down_theirs, preferred_element_type=jnp.float32
        ).astype(jnp.bfloat16)
        pair = (part_own.astype(jnp.float32) + part_from_other.astype(jnp.float32)).astype(jnp.bfloat16)
        summed = direct_scatter(ring_scatter(pair, outer_ring).astype(jnp.bfloat16), inner_ring).astype(jnp.bfloat16)
        summed = summed.astype(jnp.float32) + sum(
            swapped(summed, "section", 2 * mask).astype(jnp.float32) for mask in range(1, x_count)
        )
        full_half = (current + summed.astype(jnp.float32)).astype(jnp.bfloat16)
        block = lax.dynamic_index_in_dim(
            full_half.reshape(row_count, x_count, piece_width), xpos, 1, keepdims=False
        )
        return full_half, block

    blocks = []
    received = None
    for tick_index in range(tick_count):
        if tick_index == 0:
            current, square_sum = from_tokens(0)
        elif tick_index >= piece_count:
            current, square_sum = from_received(received)
        else:
            first_current, first_sum = from_tokens(tick_index)
            later_current, later_sum = from_received(received)
            is_first = section_layer == 0
            current = jnp.where(is_first, first_current, later_current)
            square_sum = jnp.where(is_first, first_sum, later_sum)
        layers = [layer for layer in range(LAYERS) if 0 <= tick_index - layer < piece_count]
        full_half, block = tick(current, square_sum, layers)
        blocks.append(block)
        if tick_index < tick_count - 1:
            received = shifted(full_half, "section", split)

    stacked = jnp.stack(blocks, axis=0)
    outputs = []
    for micro_index in range(micro_count):
        parts = [
            lax.dynamic_index_in_dim(stacked, micro_index * PIECES + part + section_layer, 0, keepdims=False)
            for part in range(PIECES)
        ]
        outputs.append(jnp.concatenate(parts, axis=0))
    return jnp.stack(outputs, axis=0)[None]


def solution(mesh):
    in_specs = (
        P(None, "tp", None),
        P(),
        P("section", None, "tp"),
        P("section", None, "tp"),
        P("section", "tp", None),
    )
    out_specs = P("section", None, "tp", None)
    return jax.shard_map(body, mesh=mesh, in_specs=in_specs, out_specs=out_specs, check_vma=False)
```

```python
import jax
import jax.numpy as jnp
from jax import lax
from jax.sharding import PartitionSpec as P

LAYERS = 2
PIECES = 1


epsilon = 1e-05


def swapped(value, axis, mask):
    pairs = [(source, source ^ mask) for source in range(lax.axis_size(axis))]
    return lax.ppermute(value, axis, pairs)


def tp_ring(value, inner, outer, stage, step):
    pairs = []
    for source in range(inner * outer):
        high, low = divmod(source, inner)
        if stage == "inner":
            target = high * inner + (low + step) % inner
        else:
            target = ((high + step) % outer) * inner + low
        pairs.append((source, target))
    return lax.ppermute(value, "tp", pairs)


def ring_gather(block, ring):
    half = block.shape[1] // 2
    from_left = ring(block, 1)
    from_right = ring(block, -1)
    opposite = jnp.concatenate(
        [ring(from_left[:, :half], 1), ring(from_right[:, half:], -1)], axis=1
    )
    return jnp.concatenate([block, from_right, opposite, from_left], axis=0)


def ring_scatter(groups, ring):
    rows = groups.shape[0] // 4
    half = groups.shape[1] // 2
    own, plus, opposite, minus = (groups[i * rows:(i + 1) * rows] for i in range(4))
    early_left = ring(opposite[:, :half], 1).astype(jnp.float32)
    early_right = ring(opposite[:, half:], -1).astype(jnp.float32)
    to_right = jnp.concatenate(
        [(plus[:, :half].astype(jnp.float32) + early_left).astype(jnp.bfloat16), plus[:, half:]], axis=1
    )
    to_left = jnp.concatenate(
        [minus[:, :half], (minus[:, half:].astype(jnp.float32) + early_right).astype(jnp.bfloat16)], axis=1
    )
    return (
        own.astype(jnp.float32)
        + ring(to_right, 1).astype(jnp.float32)
        + ring(to_left, -1).astype(jnp.float32)
    )


def direct_gather(block, ring):
    return jnp.concatenate([block, ring(block, -1), ring(block, 2), ring(block, 1)], axis=0)


def direct_scatter(groups, ring):
    rows = groups.shape[0] // 4
    own, plus, opposite, minus = (groups[i * rows:(i + 1) * rows] for i in range(4))
    return (
        own.astype(jnp.float32)
        + ring(plus, 1).astype(jnp.float32)
        + ring(opposite, 2).astype(jnp.float32)
        + ring(minus, -1).astype(jnp.float32)
    )


def shifted(value, axis, steps):
    count = lax.axis_size(axis)
    return lax.ppermute(value, axis, [(source, source + steps) for source in range(count - steps)])


def body(tokens, norm_gains, w_gate, w_up, w_down):
    section_count = lax.axis_size("section")
    split = section_count // LAYERS
    bit_count = split.bit_length() - 1
    position = lax.axis_index("section")
    section_layer = position // split
    member = position % split
    core = member % 2
    xpos = member // 2
    x_count = split // 2

    tp_count = lax.axis_size("tp")
    inner = 4
    outer = tp_count // inner

    def inner_ring_for(layers):
        def ring(value, step):
            pairs = []
            for section in range(section_count):
                if section // split not in layers:
                    continue
                for source in range(tp_count):
                    high, low = divmod(source, inner)
                    target = high * inner + (low + step) % inner
                    pairs.append((section * tp_count + source, section * tp_count + target))
            return lax.ppermute(value, ("section", "tp"), pairs)
        return ring

    def group_permute(value, layers, mapping):
        pairs = []
        for section in range(section_count):
            if section // split not in layers:
                continue
            for source in range(tp_count):
                to_section, target = mapping(section, source)
                pairs.append((section * tp_count + source, to_section * tp_count + target))
        return lax.ppermute(value, ("section", "tp"), pairs)

    def outer_ring_for(layers):
        def ring(value, step):
            return group_permute(
                value, layers, lambda s, t: (s, ((t // inner + step) % outer) * inner + t % inner)
            )
        return ring

    def swapped_in(value, layers, mask):
        return group_permute(value, layers, lambda s, t: (s ^ mask, t))

    micro_count, tok_dev, model_width = tokens.shape
    piece_width = model_width // split
    half_width = model_width // 2
    row_count = tok_dev // PIECES
    piece_count = micro_count * PIECES
    tick_count = piece_count + LAYERS - 1

    def pick(value, axis, which):
        shape = value.shape
        grouped = value.reshape(shape[:axis] + (x_count, 2, piece_width) + shape[axis + 1:])
        chosen = lax.dynamic_index_in_dim(grouped, which, axis + 1, keepdims=False)
        return chosen.reshape(shape[:axis] + (half_width,) + shape[axis + 1:])

    other = 1 - core
    gate_own = pick(w_gate[0], 0, core)
    gate_other = pick(w_gate[0], 0, other)
    up_own = pick(w_up[0], 0, core)
    up_other = pick(w_up[0], 0, other)
    down_own = pick(w_down[0], 1, core)
    down_other = pick(w_down[0], 1, other)
    gate_both = jnp.concatenate([gate_own, swapped(gate_other, "section", 1)], axis=1)
    up_both = jnp.concatenate([up_own, swapped(up_other, "section", 1)], axis=1)
    down_theirs = swapped(down_other, "section", 1)
    unit_count = gate_own.shape[1]
    norm_gain = lax.dynamic_index_in_dim(norm_gains, section_layer, 0, keepdims=False)
    gain_own = pick(norm_gain, 0, core)

    def from_tokens(piece_index):
        micro_index, part = divmod(piece_index, PIECES)
        rows = tokens[micro_index, part * row_count:(part + 1) * row_count].astype(jnp.float32)
        return pick(rows, 1, core), jnp.sum(rows * rows, axis=1, keepdims=True)

    def from_received(received):
        current = received.astype(jnp.float32)
        own_sq = jnp.sum(current * current, axis=1, keepdims=True)
        return current, own_sq + swapped(own_sq, "section", 1)

    def tick(current, square_sum, layers):
        inner_ring = inner_ring_for(layers)
        outer_ring = outer_ring_for(layers)
        inv_rms = lax.rsqrt(square_sum / model_width + epsilon)
        normed = (current * inv_rms * gain_own).astype(jnp.bfloat16)
        gathered = ring_gather(direct_gather(normed, inner_ring), outer_ring)
        gate_terms = jnp.dot(gathered, gate_both, preferred_element_type=jnp.float32)
        up_terms = jnp.dot(gathered, up_both, preferred_element_type=jnp.float32)
        terms_from_other = swapped_in(
            jnp.concatenate([gate_terms[:, unit_count:], up_terms[:, unit_count:]], axis=1), layers, 1
        )
        gate_proj = gate_terms[:, :unit_count] + terms_from_other[:, :unit_count]
        up_proj = up_terms[:, :unit_count] + terms_from_other[:, unit_count:]
        active = (jax.nn.silu(gate_proj) * up_proj).astype(jnp.bfloat16)
        active_from_other = swapped_in(active, layers, 1)
        part_own = jnp.dot(active, down_own, preferred_element_type=jnp.float32).astype(jnp.bfloat16)
        part_from_other = jnp.dot(
            active_from_other, down_theirs, preferred_element_type=jnp.float32
        ).astype(jnp.bfloat16)
        pair = (part_own.astype(jnp.float32) + part_from_other.astype(jnp.float32)).astype(jnp.bfloat16)
        summed = direct_scatter(ring_scatter(pair, outer_ring).astype(jnp.bfloat16), inner_ring).astype(jnp.bfloat16)
        summed = summed.astype(jnp.float32) + sum(
            swapped_in(summed, layers, 2 * mask).astype(jnp.float32) for mask in range(1, x_count)
        )
        full_half = (current + summed.astype(jnp.float32)).astype(jnp.bfloat16)
        block = lax.dynamic_index_in_dim(
            full_half.reshape(row_count, x_count, piece_width), xpos, 1, keepdims=False
        )
        return full_half, block

    blocks = []
    received = None
    for tick_index in range(tick_count):
        if tick_index == 0:
            current, square_sum = from_tokens(0)
        elif tick_index >= piece_count:
            current, square_sum = from_received(received)
        else:
            first_current, first_sum = from_tokens(tick_index)
            later_current, later_sum = from_received(received)
            is_first = section_layer == 0
            current = jnp.where(is_first, first_current, later_current)
            square_sum = jnp.where(is_first, first_sum, later_sum)
        layers = [layer for layer in range(LAYERS) if 0 <= tick_index - layer < piece_count]
        full_half, block = tick(current, square_sum, layers)
        blocks.append(block)
        if tick_index < tick_count - 1:
            received = shifted(full_half, "section", split)

    stacked = jnp.stack(blocks, axis=0)
    outputs = []
    for micro_index in range(micro_count):
        parts = [
            lax.dynamic_index_in_dim(stacked, micro_index * PIECES + part + section_layer, 0, keepdims=False)
            for part in range(PIECES)
        ]
        outputs.append(jnp.concatenate(parts, axis=0))
    return jnp.stack(outputs, axis=0)[None]


def solution(mesh):
    in_specs = (
        P(None, "tp", None),
        P(),
        P("section", None, "tp"),
        P("section", None, "tp"),
        P("section", "tp", None),
    )
    out_specs = P("section", None, "tp", None)
    return jax.shard_map(body, mesh=mesh, in_specs=in_specs, out_specs=out_specs, check_vma=False)
```
